512 devices in a mesh: sect: 8 (over x, y_hi), blk: 64 (over z, y_lo, core).
Axes of the slice: x: 4, y: 4 (y_hi: 2, y_lo: 2; y = y_hi * 2 + y_lo), z: 16, core: 2. Of those that a mesh axis runs over, the one named last changes fastest.
Arguments:
- bits: int32 [8, 1024], P('sect', 'blk'), may hold values from 0 to 1
- labels: int32 [128], replicated, may hold values from 0 to 127, each once
- left: bfloat16 [1024, 16384], P('blk')
- tensors: bfloat16 [8, 2, 128, 128, 128], P('sect', None, 'blk')
Outputs:
- prob: float32 [8, 1024], P('sect', 'blk')
- logprob: float32 [8, 1024], P('sect', 'blk')
The draws below stay inside these ranges and needn't reach their ends.
Inputs may be any that keep to these rules, and one draw needn't show every extreme that they name: Every charge labels exactly one block.
All inputs are finite; a program needn't handle non-finite values.
Results may differ from the reference program's by a relative error of at most 0.0003.
Values may be sent and summed in bfloat16 or wider, within the bound.
No kernel may reach another device: no remote copies, remote signals or barrier semaphores. Data moves between devices by JAX's collectives and lax.ppermute only.
A program may use at most 64 MiB of HBM per device.

```python
import math
import jax
import jax.numpy as jnp
from jax import lax

D = 16384
BLOCK = 128
NB = 128
SAMPLES = 1024
SITES = 8


def draw_left(key, part):
    key_base = jax.random.fold_in(key, 21)
    key_block = jax.random.fold_in(key, 22)
    key_rough = jax.random.fold_in(key, 23)
    shape = (SAMPLES, NB, BLOCK)
    base = jax.random.normal(key_base, shape, jnp.float32)
    block_scale = jnp.exp(jax.random.uniform(key_block, (NB,), jnp.float32, 0.0, math.log(10.0)))
    rough = jnp.exp(jax.random.uniform(key_rough, (SAMPLES, NB), jnp.float32, math.log(0.5), math.log(2.0)))
    value = base * block_scale[None, :, None] * rough[:, :, None]
    return value.reshape(SAMPLES, D).astype(jnp.bfloat16)


def draw_tensors(key, part):
    key_base = jax.random.fold_in(key, 11)
    key_scale = jax.random.fold_in(key, 12)
    shape = (SITES, 2, NB, BLOCK, BLOCK)
    base = jax.random.normal(key_base, shape, jnp.float32)
    rise = jnp.exp(math.log(3.0) * jnp.arange(NB, dtype=jnp.float32) / (NB - 1))
    spread = jnp.exp(jax.random.uniform(key_scale, (SITES, 2, NB), jnp.float32, math.log(0.5), math.log(5.0)))
    factor = rise[None, None, :] * spread / math.sqrt(BLOCK)
    return (base * factor[:, :, :, None, None]).astype(jnp.bfloat16)


def plant(result, rng, least, high):
    longest = result.shape.index(max(result.shape))
    spots = []
    for shift in (0, 1):
        where = [jax.random.randint(jax.random.fold_in(rng, axis), (), 0, length) for axis, length in enumerate(result.shape)]
        where[longest] = (where[longest] + shift) % result.shape[longest]
        spots.append(tuple(where))
    return result.at[spots[0]].set(least).at[spots[1]].set(high)


def setup_inputs(seed: int = 0) -> dict:
    streams_of = jax.random.split(jax.random.key(seed), 5)
    bits = plant(jax.random.randint(streams_of[0], (SITES, SAMPLES), 0, 2), jax.random.fold_in(streams_of[0], 1), 0, 1).astype(jnp.int32)
    labels = jax.random.permutation(streams_of[1], NB).astype(jnp.int32)
    left = draw_left(jax.random.fold_in(streams_of[4], 71), 0)
    tensors = draw_tensors(jax.random.fold_in(streams_of[4], 71), 0)
    return dict(bits=bits, labels=labels, left=left, tensors=tensors)


def charge_order(labels, left):
    index = jnp.arange(NB, dtype=jnp.int32)
    match = labels[None, :] == index[:, None]
    source = lax.optimization_barrier(jnp.sum(jnp.where(match, index[None, :], 0), axis=1)).astype(jnp.int32)
    blocks = left.reshape(SAMPLES, NB, BLOCK)
    return jnp.take(blocks, source, axis=1).reshape(SAMPLES, D)

def reference(bits, labels, left, tensors):
    state = charge_order(labels, left).astype(jnp.float32)
    total = jnp.zeros((SAMPLES,), jnp.float32)
    probs = []
    logs = []
    for site in range(SITES):
        blocks = state.reshape(SAMPLES, NB, BLOCK)
        image = jnp.einsum('nck,bckl->bncl', blocks, tensors[site].astype(jnp.float32), precision=lax.Precision.HIGHEST)
        stay = image[0]
        raised = jnp.roll(image[1], 1, axis=1)
        norm_zero = lax.optimization_barrier(jnp.sum(stay * stay, axis=(1, 2)))
        norm_one = lax.optimization_barrier(jnp.sum(raised * raised, axis=(1, 2)))
        choose = bits[site] == 1
        chosen_norm = jnp.where(choose, norm_one, norm_zero)
        prob = chosen_norm / (norm_zero + norm_one)
        total = total + jnp.log(prob)
        chosen = jnp.where(choose[:, None, None], raised, stay)
        scaled = chosen * lax.rsqrt(chosen_norm / D + 1e-06)[:, None, None]
        state = scaled.reshape(SAMPLES, D)
        probs.append(prob)
        logs.append(total)
    return (jnp.stack(probs), jnp.stack(logs))
```

```python
import jax
import jax.numpy as jnp
from jax import lax
from jax.sharding import PartitionSpec as P


def charge_blocks(labels, rows, block):
    count_blocks = labels.shape[0]
    blocks = rows.reshape(rows.shape[0], count_blocks, block)
    index = jnp.arange(count_blocks, dtype=jnp.int32)
    pick = (labels[None, :] == index[:, None]).astype(blocks.dtype)
    ordered = jnp.einsum("ci,rik->rck", pick, blocks, preferred_element_type=jnp.float32)
    return ordered.astype(blocks.dtype)


def body(bits, labels, left, tensors):
    sect = lax.axis_index("sect")
    blk = lax.axis_index("blk")
    n_sect = lax.axis_size("sect")
    n_blk = lax.axis_size("blk")
    block = tensors.shape[-1]
    count_blocks = labels.shape[0]
    width = count_blocks * block
    sites = bits.shape[0] * n_sect
    per_blk = left.shape[0]
    pick_rows = per_blk // n_sect
    local_blocks = tensors.shape[2]

    weights = lax.all_gather(tensors[0], "sect", axis=0, tiled=False)

    all_bits = lax.all_gather(bits, ("sect", "blk"), axis=0, tiled=False)
    all_bits = all_bits.reshape(n_sect, n_blk, bits.shape[0], per_blk)[:, :, 0, :]
    all_bits = all_bits.reshape(sites, n_blk, n_sect, pick_rows)
    group_bits = lax.dynamic_index_in_dim(all_bits, sect, 2, keepdims=False)
    group_bits = group_bits.reshape(sites, n_blk * pick_rows)

    mine = lax.dynamic_slice_in_dim(left, sect * pick_rows, pick_rows, 0)
    ordered = charge_blocks(labels, mine, block)
    ordered = ordered.reshape(pick_rows, n_blk, local_blocks, block)
    spread = lax.all_to_all(ordered, "blk", 1, 1, tiled=False)
    rows = n_blk * pick_rows
    state = jnp.transpose(spread, (1, 0, 2, 3)).reshape(rows, local_blocks, block)
    state = state.astype(jnp.float32)

    total = jnp.zeros((rows,), jnp.float32)
    shift = [(j, (j + 1) % n_blk) for j in range(n_blk)]
    probs = []
    logs = []
    for site in range(sites):
        image = jnp.einsum(
            "rck,bckl->brcl",
            state,
            weights[site].astype(jnp.float32),
            preferred_element_type=jnp.float32,
            precision=lax.Precision.HIGHEST,
        )
        stay = image[0]
        rise = image[1]
        part = jnp.stack([jnp.sum(stay * stay, axis=(1, 2)), jnp.sum(rise * rise, axis=(1, 2))])
        norms = lax.psum(part, "blk")
        came = lax.ppermute(rise[:, local_blocks - 1], "blk", shift)
        raised = jnp.concatenate([came[:, None], rise[:, : local_blocks - 1]], axis=1)
        norm_zero = norms[0]
        norm_one = norms[1]
        choose = group_bits[site] == 1
        chosen_norm = jnp.where(choose, norm_one, norm_zero)
        prob = chosen_norm / (norm_zero + norm_one)
        total = total + jnp.log(prob)
        probs.append(prob)
        logs.append(total)
        if site + 1 < sites:
            chosen = jnp.where(choose[:, None, None], raised, stay)
            state = chosen * lax.rsqrt(chosen_norm / width + 1e-06)[:, None, None]

    result = jnp.stack([jnp.stack(probs), jnp.stack(logs)], axis=1)
    result = result.reshape(sites, 2, n_blk, pick_rows)
    result = lax.dynamic_index_in_dim(result, blk, 2, keepdims=False)
    result = result.reshape(n_sect, bits.shape[0], 2, pick_rows)
    back = lax.all_to_all(result, "sect", 0, 0, tiled=False)
    back = back[:, 0]
    out = jnp.transpose(back, (1, 0, 2)).reshape(2, bits.shape[0], n_sect * pick_rows)
    return (out[0], out[1])


def solution(mesh):
    in_specs = (P("sect", "blk"), P(), P("blk", None), P("sect", None, "blk", None, None))
    out_specs = (P("sect", "blk"), P("sect", "blk"))
    return jax.shard_map(body, mesh=mesh, in_specs=in_specs, out_specs=out_specs, check_vma=False)
```

```python
import jax
import jax.numpy as jnp
from jax import lax
from jax.sharding import PartitionSpec as P


def charge_order(labels, left, block):
    count_blocks = labels.shape[0]
    samples_here = left.shape[0]
    blocks = left.reshape(samples_here, count_blocks, block)
    index = jnp.arange(count_blocks, dtype=jnp.int32)
    pick = (labels[None, :] == index[:, None]).astype(jnp.bfloat16)
    ordered = jnp.einsum("ci,rik->rck", pick, blocks, preferred_element_type=jnp.float32)
    return ordered.astype(jnp.bfloat16)


def body(bits, labels, left, tensors):
    block = tensors.shape[-1]
    count_blocks = labels.shape[0]
    width = count_blocks * block
    rows = bits.shape[1]
    segment = lax.axis_index("sect")
    segments = lax.axis_size("sect")
    whole = lax.all_gather(tensors, "blk", axis=2, tiled=True)[0]
    choose = bits[0] == 1

    state = charge_order(labels, left, block).astype(jnp.float32)
    total = jnp.zeros((rows,), jnp.float32)
    prob_out = jnp.zeros((rows,), jnp.float32)
    log_out = jnp.zeros((rows,), jnp.float32)
    for step in range(segments):
        rounded = lax.reduce_precision(state, exponent_bits=8, mantissa_bits=7)
        high = rounded.astype(jnp.bfloat16)
        low = (state - rounded).astype(jnp.bfloat16)
        parts = jnp.concatenate([high, low], axis=0).reshape(2 * rows, count_blocks, block)
        both = jnp.einsum("rck,bckl->brcl", parts, whole, preferred_element_type=jnp.float32)
        image = both[:, :rows] + both[:, rows:]
        stay = image[0]
        raised = jnp.roll(image[1], 1, axis=1)
        norm_zero = jnp.sum(stay * stay, axis=(1, 2))
        norm_one = jnp.sum(raised * raised, axis=(1, 2))
        chosen_norm = jnp.where(choose, norm_one, norm_zero)
        prob = chosen_norm / (norm_zero + norm_one)
        total = total + jnp.log(prob)
        here = segment == step
        prob_out = jnp.where(here, prob, prob_out)
        log_out = jnp.where(here, total, log_out)
        if step + 1 < segments:
            chosen = jnp.where(choose[:, None, None], raised, stay)
            scaled = chosen * lax.rsqrt(chosen_norm / width + 1e-06)[:, None, None]
            extra = jnp.zeros((1, width), jnp.float32).at[0, :rows].set(total)
            sent = jnp.concatenate([scaled.reshape(rows, width), extra], axis=0)
            came = lax.ppermute(sent, "sect", [(step, step + 1)])
            state = came[:rows]
            total = came[rows, :rows]
    return (prob_out[None], log_out[None])


def solution(mesh):
    in_specs = (P("sect", "blk"), P(), P("blk", None), P("sect", None, "blk", None, None))
    out_specs = (P("sect", "blk"), P("sect", "blk"))
    return jax.shard_map(body, mesh=mesh, in_specs=in_specs, out_specs=out_specs, check_vma=False)
```

```python
import jax
import jax.numpy as jnp
from jax import lax
from jax.sharding import PartitionSpec as P

MICRO = 2


def charge_order(labels, left, block):
    count_blocks = labels.shape[0]
    samples_here = left.shape[0]
    blocks = left.reshape(samples_here, count_blocks, block)
    index = jnp.arange(count_blocks, dtype=jnp.int32)
    pick = (labels[None, :] == index[:, None]).astype(jnp.bfloat16)
    ordered = jnp.einsum("ci,rik->rck", pick, blocks, preferred_element_type=jnp.float32)
    return ordered.astype(jnp.bfloat16)


def site_images(state, weights, block):
    count_rows = state.shape[0]
    rounded = lax.reduce_precision(state, exponent_bits=8, mantissa_bits=7)
    high = rounded.astype(jnp.bfloat16)
    low = (state - rounded).astype(jnp.bfloat16)
    parts = jnp.concatenate([high, low], axis=0).reshape(2 * count_rows, weights.shape[1], block)
    both = jnp.einsum("rck,bckl->brcl", parts, weights, preferred_element_type=jnp.float32)
    return both[:, :count_rows] + both[:, count_rows:]


def body(bits, labels, left, tensors):
    block = tensors.shape[-1]
    count_blocks = labels.shape[0]
    width = count_blocks * block
    rows = bits.shape[1]
    segment = lax.axis_index("sect")
    segments = lax.axis_size("sect")
    n_blk = lax.axis_size("blk")
    whole = lax.all_gather(tensors, "blk", axis=2, tiled=True)[0]

    flip = [(b, b ^ 2) for b in range(n_blk)]
    odd = segment % 2 == 1
    carried_bits = jnp.where(odd, lax.ppermute(bits, "blk", flip), bits)[0]
    hop = [(s * n_blk + b, (s + 1) * n_blk + (b ^ 2)) for s in range(segments - 1) for b in range(n_blk)]

    count = MICRO
    mrows = rows // count
    start_rows = charge_order(labels, left, block).astype(jnp.float32).reshape(count, mrows, width)
    site_bits = (carried_bits == 1).reshape(count, mrows)

    def advance(state, choose):
        image = site_images(state, whole, block)
        stay = image[0]
        raised = jnp.roll(image[1], 1, axis=1)
        norm_zero = jnp.sum(stay * stay, axis=(1, 2))
        norm_one = jnp.sum(raised * raised, axis=(1, 2))
        chosen_norm = jnp.where(choose, norm_one, norm_zero)
        prob = chosen_norm / (norm_zero + norm_one)
        chosen = jnp.where(choose[:, None, None], raised, stay)
        scaled = chosen * lax.rsqrt(chosen_norm / width + 1e-06)[:, None, None]
        return (prob, scaled.reshape(mrows, width))

    def one_step(step, carry, send):
        state, total, prob_out, log_out = carry
        group = step - segment
        valid = (group >= 0) & (group < count)
        slot = jnp.clip(group, 0, count - 1)
        first = segment == 0
        state = jnp.where(first, lax.dynamic_index_in_dim(start_rows, slot, 0, keepdims=False), state)
        total = jnp.where(first, jnp.zeros_like(total), total)
        choose = lax.dynamic_index_in_dim(site_bits, slot, 0, keepdims=False)
        prob, next_state = advance(state, choose)
        total = total + jnp.log(prob)
        old_prob = lax.dynamic_index_in_dim(prob_out, slot, 0, keepdims=False)
        old_log = lax.dynamic_index_in_dim(log_out, slot, 0, keepdims=False)
        prob_out = lax.dynamic_update_index_in_dim(prob_out, jnp.where(valid, prob, old_prob), slot, 0)
        log_out = lax.dynamic_update_index_in_dim(log_out, jnp.where(valid, total, old_log), slot, 0)
        if send:
            extra = jnp.zeros((1, width), jnp.float32).at[0, :mrows].set(total)
            sent = jnp.concatenate([next_state, extra], axis=0)
            came = lax.ppermute(sent, ("sect", "blk"), hop)
            state = came[:mrows]
            total = came[mrows, :mrows]
        return (state, total, prob_out, log_out)

    empty = jnp.zeros((count, mrows), jnp.float32)
    init = (start_rows[0], jnp.zeros((mrows,), jnp.float32), empty, empty)
    steps = count + segments - 1
    carry = lax.fori_loop(0, steps - 1, lambda step, carry: one_step(step, carry, True), init)
    carry = one_step(steps - 1, carry, False)
    result = jnp.stack([carry[2].reshape(rows), carry[3].reshape(rows)])
    result = jnp.where(odd, lax.ppermute(result, "blk", flip), result)
    return (result[0][None], result[1][None])


def solution(mesh):
    in_specs = (P("sect", "blk"), P(), P("blk", None), P("sect", None, "blk", None, None))
    out_specs = (P("sect", "blk"), P("sect", "blk"))
    return jax.shard_map(body, mesh=mesh, in_specs=in_specs, out_specs=out_specs, check_vma=False)
```

```python
import jax
import jax.numpy as jnp
from jax import lax
from jax.sharding import Mesh
from jax.sharding import PartitionSpec as P

PARTS = 8


def charge_order(labels, rows, block):
    count_blocks = labels.shape[0]
    blocks = rows.reshape(rows.shape[0], count_blocks, block)
    index = jnp.arange(count_blocks, dtype=jnp.int32)
    pick = (labels[None, :] == index[:, None]).astype(blocks.dtype)
    ordered = jnp.einsum("ci,rik->rck", pick, blocks, preferred_element_type=jnp.float32)
    return ordered.astype(blocks.dtype)


def site_images(state, weights):
    count_rows = state.shape[0]
    rounded = lax.reduce_precision(state, exponent_bits=8, mantissa_bits=7)
    high = rounded.astype(jnp.bfloat16)
    low = (state - rounded).astype(jnp.bfloat16)
    parts = jnp.concatenate([high, low], axis=0)
    both = jnp.einsum("rck,bckl->brcl", parts, weights, preferred_element_type=jnp.float32)
    return both[:, :count_rows] + both[:, count_rows:]


def body(bits, labels, left, tensors):
    sect = lax.axis_index("sect")
    bhi = lax.axis_index("bhi")
    n_sect = lax.axis_size("sect")
    n_hi = lax.axis_size("bhi")
    n_lo = lax.axis_size("blo")
    block = tensors.shape[-1]
    count_blocks = labels.shape[0]
    width = count_blocks * block
    sites = bits.shape[0] * n_sect
    per_dev = left.shape[0]
    pick = per_dev // n_sect
    mine = count_blocks // n_hi

    slabs = lax.all_gather(tensors[0], "sect", axis=0, tiled=False)

    pieces = bits[0].reshape(n_sect, pick)
    pieces = lax.all_to_all(pieces, "sect", 0, 0, tiled=False)
    carried_bits = lax.all_gather(pieces, "bhi", axis=0, tiled=False)
    carried_bits = jnp.transpose(carried_bits, (1, 0, 2)).reshape(sites, n_hi * pick)

    rows = lax.dynamic_slice_in_dim(left, sect * pick, pick, 0)
    ordered = charge_order(labels, rows, block).reshape(pick, n_hi, mine, block)
    spread = lax.all_to_all(ordered, "bhi", 1, 1, tiled=False)
    count_rows = n_hi * pick
    state = jnp.transpose(spread, (1, 0, 2, 3)).reshape(count_rows, mine, block).astype(jnp.float32)

    total = jnp.zeros((count_rows,), jnp.float32)
    shift = [(q, (q + 1) % n_hi) for q in range(n_hi)]
    probs = []
    logs = []
    for site in range(sites):
        weights = lax.all_gather(slabs[site], "blo", axis=1, tiled=True)
        image = site_images(state, weights)
        stay = image[0]
        rise = image[1]
        part = jnp.stack([jnp.sum(stay * stay, axis=(1, 2)), jnp.sum(rise * rise, axis=(1, 2))])
        norms = lax.psum(part, "bhi")
        came = lax.ppermute(rise[:, mine - 1], "bhi", shift)
        raised = jnp.concatenate([came[:, None], rise[:, : mine - 1]], axis=1)
        norm_zero = norms[0]
        norm_one = norms[1]
        choose = carried_bits[site] == 1
        chosen_norm = jnp.where(choose, norm_one, norm_zero)
        prob = chosen_norm / (norm_zero + norm_one)
        total = total + jnp.log(prob)
        probs.append(prob)
        logs.append(total)
        if site + 1 < sites:
            chosen = jnp.where(choose[:, None, None], raised, stay)
            state = chosen * lax.rsqrt(chosen_norm / width + 1e-06)[:, None, None]

    result = jnp.stack([jnp.stack(probs), jnp.stack(logs)], axis=1)
    result = lax.dynamic_slice_in_dim(result, bhi * pick, pick, 2)
    back = lax.all_to_all(result, "sect", 0, 0, tiled=False)
    out = jnp.transpose(back, (1, 0, 2)).reshape(2, bits.shape[0], n_sect * pick)
    return (out[0], out[1])


def solution(mesh):
    n_sect, n_blk = mesh.devices.shape
    fine = Mesh(mesh.devices.reshape(n_sect, PARTS, n_blk // PARTS), ("sect", "bhi", "blo"))
    blk = ("bhi", "blo")
    in_specs = (P("sect", blk), P(), P(blk, None), P("sect", None, blk, None, None))
    out_specs = (P("sect", blk), P("sect", blk))
    return jax.shard_map(body, mesh=fine, in_specs=in_specs, out_specs=out_specs, check_vma=False)
```

```python
import jax
import jax.numpy as jnp
from jax import lax
from jax.sharding import Mesh
from jax.sharding import PartitionSpec as P

PARTS = 8


def charge_order(labels, rows, block):
    count_blocks = labels.shape[0]
    blocks = rows.reshape(rows.shape[0], count_blocks, block)
    index = jnp.arange(count_blocks, dtype=jnp.int32)
    pick = (labels[None, :] == index[:, None]).astype(blocks.dtype)
    ordered = jnp.einsum("ci,rik->rck", pick, blocks, preferred_element_type=jnp.float32)
    return ordered.astype(blocks.dtype)


def site_images(state, weights):
    count_rows = state.shape[0]
    rounded = lax.reduce_precision(state, exponent_bits=8, mantissa_bits=7)
    high = rounded.astype(jnp.bfloat16)
    low = (state - rounded).astype(jnp.bfloat16)
    parts = jnp.concatenate([high, low], axis=0)
    both = jnp.einsum("rck,bckl->brcl", parts, weights, preferred_element_type=jnp.float32)
    return both[:, :count_rows] + both[:, count_rows:]


def body(bits, labels, left, tensors):
    sect = lax.axis_index("sect")
    bhi = lax.axis_index("bhi")
    n_sect = lax.axis_size("sect")
    n_hi = lax.axis_size("bhi")
    n_lo = lax.axis_size("blo")
    block = tensors.shape[-1]
    count_blocks = labels.shape[0]
    width = count_blocks * block
    sites = bits.shape[0] * n_sect
    per_dev = left.shape[0]
    pick = per_dev // n_sect
    mine = count_blocks // n_hi

    slabs = lax.all_gather(tensors[0], "sect", axis=0, tiled=False)

    pieces = lax.all_to_all(bits[0].reshape(n_sect, pick), "sect", 0, 0, tiled=False)
    row_bits = jnp.transpose(pieces).astype(left.dtype)

    rows = lax.dynamic_slice_in_dim(left, sect * pick, pick, 0)
    ordered = charge_order(labels, rows, block).reshape(pick, n_hi, mine * block)
    tagged = jnp.broadcast_to(row_bits[:, None, :], (pick, n_hi, sites))
    spread = lax.all_to_all(jnp.concatenate([ordered, tagged], axis=2), "bhi", 1, 1, tiled=False)
    count_rows = n_hi * pick
    spread = jnp.transpose(spread, (1, 0, 2)).reshape(count_rows, mine * block + sites)
    state = spread[:, : mine * block].reshape(count_rows, mine, block).astype(jnp.float32)
    carried_bits = jnp.transpose(spread[:, mine * block :])

    total = jnp.zeros((count_rows,), jnp.float32)
    shift = [(q, (q + 1) % n_hi) for q in range(n_hi)]
    probs = []
    logs = []
    for site in range(sites):
        weights = lax.all_gather(slabs[site], "blo", axis=1, tiled=True)
        image = site_images(state, weights)
        stay = image[0]
        rise = image[1]
        part = jnp.stack([jnp.sum(stay * stay, axis=(1, 2)), jnp.sum(rise * rise, axis=(1, 2))])
        norms = lax.psum(part, "bhi")
        came = lax.ppermute(rise[:, mine - 1], "bhi", shift)
        raised = jnp.concatenate([came[:, None], rise[:, : mine - 1]], axis=1)
        norm_zero = norms[0]
        norm_one = norms[1]
        choose = carried_bits[site] == 1
        chosen_norm = jnp.where(choose, norm_one, norm_zero)
        prob = chosen_norm / (norm_zero + norm_one)
        total = total + jnp.log(prob)
        probs.append(prob)
        logs.append(total)
        if site + 1 < sites:
            chosen = jnp.where(choose[:, None, None], raised, stay)
            state = chosen * lax.rsqrt(chosen_norm / width + 1e-06)[:, None, None]

    result = jnp.stack([jnp.stack(probs), jnp.stack(logs)], axis=1)
    result = lax.dynamic_slice_in_dim(result, bhi * pick, pick, 2)
    back = lax.all_to_all(result, "sect", 0, 0, tiled=False)
    out = jnp.transpose(back, (1, 0, 2)).reshape(2, bits.shape[0], n_sect * pick)
    return (out[0], out[1])


def solution(mesh):
    n_sect, n_blk = mesh.devices.shape
    fine = Mesh(mesh.devices.reshape(n_sect, PARTS, n_blk // PARTS), ("sect", "bhi", "blo"))
    blk = ("bhi", "blo")
    in_specs = (P("sect", blk), P(), P(blk, None), P("sect", None, blk, None, None))
    out_specs = (P("sect", blk), P("sect", blk))
    return jax.shard_map(body, mesh=fine, in_specs=in_specs, out_specs=out_specs, check_vma=False)
```

```python
import jax
import jax.numpy as jnp
from jax import lax
from jax.sharding import Mesh
from jax.sharding import PartitionSpec as P

PARTS = 8


def charge_order(labels, rows, block):
    count_blocks = labels.shape[0]
    blocks = rows.reshape(rows.shape[0], count_blocks, block)
    index = jnp.arange(count_blocks, dtype=jnp.int32)
    pick = (labels[None, :] == index[:, None]).astype(blocks.dtype)
    ordered = jnp.einsum("ci,rik->rck", pick, blocks, preferred_element_type=jnp.float32)
    return ordered.astype(blocks.dtype)


def site_images(state, weights):
    count_rows = state.shape[0]
    rounded = lax.reduce_precision(state, exponent_bits=8, mantissa_bits=7)
    high = rounded.astype(jnp.bfloat16)
    low = (state - rounded).astype(jnp.bfloat16)
    parts = jnp.concatenate([high, low], axis=0)
    both = jnp.einsum("rck,bckl->brcl", parts, weights, preferred_element_type=jnp.float32)
    return both[:, :count_rows] + both[:, count_rows:]


def body(bits, labels, left, tensors):
    sect = lax.axis_index("sect")
    bhi = lax.axis_index("bhi")
    n_sect = lax.axis_size("sect")
    n_hi = lax.axis_size("bhi")
    n_lo = lax.axis_size("blo")
    block = tensors.shape[-1]
    count_blocks = labels.shape[0]
    width = count_blocks * block
    sites = bits.shape[0] * n_sect
    per_dev = left.shape[0]
    pick = per_dev // n_sect
    mine = count_blocks // n_hi

    slabs = lax.all_gather(tensors[0], "sect", axis=0, tiled=False)

    pieces = lax.all_to_all(bits[0].reshape(n_sect, pick), "sect", 0, 0, tiled=False)
    row_bits = jnp.transpose(pieces).astype(left.dtype)

    rows = lax.dynamic_slice_in_dim(left, sect * pick, pick, 0)
    ordered = charge_order(labels, rows, block).reshape(pick, n_hi, mine * block)
    tagged = jnp.broadcast_to(row_bits[:, None, :], (pick, n_hi, sites))
    spread = lax.all_to_all(jnp.concatenate([ordered, tagged], axis=2), "bhi", 1, 1, tiled=False)
    count_rows = n_hi * pick
    spread = jnp.transpose(spread, (1, 0, 2)).reshape(count_rows, mine * block + sites)
    state = spread[:, : mine * block].reshape(count_rows, mine, block).astype(jnp.float32)
    carried_bits = jnp.transpose(spread[:, mine * block :])

    total = jnp.zeros((count_rows,), jnp.float32)
    shift = [(q, (q + 1) % n_hi) for q in range(n_hi)]
    probs = []
    logs = []
    batches = [[0]] + [list(range(k, min(k + 2, sites))) for k in range(1, sites, 2)]
    gathered = {}
    for batch in batches:
        got = lax.all_gather(slabs[batch[0] : batch[-1] + 1], "blo", axis=2, tiled=True)
        for index, site in enumerate(batch):
            gathered[site] = got[index]
    for site in range(sites):
        weights = gathered[site]
        image = site_images(state, weights)
        stay = image[0]
        rise = image[1]
        part = jnp.stack([jnp.sum(stay * stay, axis=(1, 2)), jnp.sum(rise * rise, axis=(1, 2))])
        norms = lax.psum(part, "bhi")
        came = lax.ppermute(rise[:, mine - 1], "bhi", shift)
        raised = jnp.concatenate([came[:, None], rise[:, : mine - 1]], axis=1)
        norm_zero = norms[0]
        norm_one = norms[1]
        choose = carried_bits[site] == 1
        chosen_norm = jnp.where(choose, norm_one, norm_zero)
        prob = chosen_norm / (norm_zero + norm_one)
        total = total + jnp.log(prob)
        probs.append(prob)
        logs.append(total)
        if site + 1 < sites:
            chosen = jnp.where(choose[:, None, None], raised, stay)
            state = chosen * lax.rsqrt(chosen_norm / width + 1e-06)[:, None, None]

    result = jnp.stack([jnp.stack(probs), jnp.stack(logs)], axis=1)
    result = lax.dynamic_slice_in_dim(result, bhi * pick, pick, 2)
    back = lax.all_to_all(result, "sect", 0, 0, tiled=False)
    out = jnp.transpose(back, (1, 0, 2)).reshape(2, bits.shape[0], n_sect * pick)
    return (out[0], out[1])


def solution(mesh):
    n_sect, n_blk = mesh.devices.shape
    fine = Mesh(mesh.devices.reshape(n_sect, PARTS, n_blk // PARTS), ("sect", "bhi", "blo"))
    blk = ("bhi", "blo")
    in_specs = (P("sect", blk), P(), P(blk, None), P("sect", None, blk, None, None))
    out_specs = (P("sect", blk), P("sect", blk))
    return jax.shard_map(body, mesh=fine, in_specs=in_specs, out_specs=out_specs, check_vma=False)
```

```python
import jax
import jax.numpy as jnp
from jax import lax
from jax.sharding import Mesh
from jax.sharding import PartitionSpec as P

PARTS = 8


def charge_order(labels, rows, block):
    count_blocks = labels.shape[0]
    blocks = rows.reshape(rows.shape[0], count_blocks, block)
    index = jnp.arange(count_blocks, dtype=jnp.int32)
    pick = (labels[None, :] == index[:, None]).astype(blocks.dtype)
    ordered = jnp.einsum("ci,rik->rck", pick, blocks, preferred_element_type=jnp.float32)
    return ordered.astype(blocks.dtype)


def site_images(state, weights):
    count_rows = state.shape[0]
    rounded = lax.reduce_precision(state, exponent_bits=8, mantissa_bits=7)
    high = rounded.astype(jnp.bfloat16)
    low = (state - rounded).astype(jnp.bfloat16)
    parts = jnp.concatenate([high, low], axis=0)
    both = jnp.einsum("rck,bckl->brcl", parts, weights, preferred_element_type=jnp.float32)
    return both[:, :count_rows] + both[:, count_rows:]


def body(bits, labels, left, tensors):
    sect = lax.axis_index("sect")
    bhi = lax.axis_index("bhi")
    n_sect = lax.axis_size("sect")
    n_hi = lax.axis_size("bhi")
    n_lo = lax.axis_size("blo")
    block = tensors.shape[-1]
    count_blocks = labels.shape[0]
    width = count_blocks * block
    sites = bits.shape[0] * n_sect
    per_dev = left.shape[0]
    pick = per_dev // n_sect
    mine = count_blocks // n_hi

    slabs = lax.all_gather(tensors[0], "sect", axis=0, tiled=False)

    pieces = lax.all_to_all(bits[0].reshape(n_sect, pick), "sect", 0, 0, tiled=False)
    row_bits = jnp.transpose(pieces).astype(left.dtype)

    rows = lax.dynamic_slice_in_dim(left, sect * pick, pick, 0)
    ordered = charge_order(labels, rows, block).reshape(pick, n_lo, n_hi, mine // n_lo, block)
    ordered = jnp.transpose(ordered, (0, 2, 1, 3, 4)).reshape(pick, n_hi, mine * block)
    tagged = jnp.broadcast_to(row_bits[:, None, :], (pick, n_hi, sites))
    spread = lax.all_to_all(jnp.concatenate([ordered, tagged], axis=2), "bhi", 1, 1, tiled=False)
    count_rows = n_hi * pick
    spread = jnp.transpose(spread, (1, 0, 2)).reshape(count_rows, mine * block + sites)
    state = spread[:, : mine * block].reshape(count_rows, mine, block).astype(jnp.float32)
    carried_bits = jnp.transpose(spread[:, mine * block :])

    total = jnp.zeros((count_rows,), jnp.float32)
    shift = [(q, (q + 1) % n_hi) for q in range(n_hi)]
    probs = []
    logs = []
    batches = [[0]] + [list(range(k, min(k + 2, sites))) for k in range(1, sites, 2)]
    gathered = {}
    for batch in batches:
        got = lax.all_gather(slabs[batch[0] : batch[-1] + 1], "blo", axis=2, tiled=True)
        for index, site in enumerate(batch):
            gathered[site] = got[index]
    for site in range(sites):
        weights = gathered[site]
        image = site_images(state, weights)
        stay = image[0]
        rise = image[1]
        part = jnp.stack([jnp.sum(stay * stay, axis=(1, 2)), jnp.sum(rise * rise, axis=(1, 2))])
        norms = lax.psum(part, "bhi")
        rise4 = rise.reshape(count_rows, n_lo, mine // n_lo, block)
        send = rise4[:, :, mine // n_lo - 1]
        send = jnp.where(bhi == n_hi - 1, jnp.roll(send, 1, axis=1), send)
        came = lax.ppermute(send, "bhi", shift)
        raised = jnp.stack([came, rise4[:, :, 0]], axis=2).reshape(count_rows, mine, block)
        norm_zero = norms[0]
        norm_one = norms[1]
        choose = carried_bits[site] == 1
        chosen_norm = jnp.where(choose, norm_one, norm_zero)
        prob = chosen_norm / (norm_zero + norm_one)
        total = total + jnp.log(prob)
        probs.append(prob)
        logs.append(total)
        if site + 1 < sites:
            chosen = jnp.where(choose[:, None, None], raised, stay)
            state = chosen * lax.rsqrt(chosen_norm / width + 1e-06)[:, None, None]

    result = jnp.stack([jnp.stack(probs), jnp.stack(logs)], axis=1)
    result = lax.dynamic_slice_in_dim(result, bhi * pick, pick, 2)
    back = lax.all_to_all(result, "sect", 0, 0, tiled=False)
    out = jnp.transpose(back, (1, 0, 2)).reshape(2, bits.shape[0], n_sect * pick)
    return (out[0], out[1])


def solution(mesh):
    n_sect, n_blk = mesh.devices.shape
    fine = Mesh(mesh.devices.reshape(n_sect, n_blk // PARTS, PARTS), ("sect", "blo", "bhi"))
    blk = ("blo", "bhi")
    in_specs = (P("sect", blk), P(), P(blk, None), P("sect", None, blk, None, None))
    out_specs = (P("sect", blk), P("sect", blk))
    return jax.shard_map(body, mesh=fine, in_specs=in_specs, out_specs=out_specs, check_vma=False)
```

```python
import jax
import jax.numpy as jnp
from jax import lax
from jax.sharding import Mesh
from jax.sharding import PartitionSpec as P

PARTS = 8


def charge_order(labels, rows, block):
    count_blocks = labels.shape[0]
    blocks = rows.reshape(rows.shape[0], count_blocks, block)
    index = jnp.arange(count_blocks, dtype=jnp.int32)
    pick = (labels[None, :] == index[:, None]).astype(blocks.dtype)
    ordered = jnp.einsum("ci,rik->rck", pick, blocks, preferred_element_type=jnp.float32)
    return ordered.astype(blocks.dtype)


def site_images(state, weights):
    count_rows = state.shape[0]
    rounded = lax.reduce_precision(state, exponent_bits=8, mantissa_bits=7)
    high = rounded.astype(jnp.bfloat16)
    low = (state - rounded).astype(jnp.bfloat16)
    parts = jnp.concatenate([high, low], axis=0)
    both = jnp.einsum("rck,bckl->brcl", parts, weights, preferred_element_type=jnp.float32)
    return both[:, :count_rows] + both[:, count_rows:]


def body(bits, labels, left, tensors):
    sect = lax.axis_index("sect")
    bhi = lax.axis_index("bhi")
    n_sect = lax.axis_size("sect")
    n_hi = lax.axis_size("bhi")
    n_lo = lax.axis_size("blo")
    block = tensors.shape[-1]
    count_blocks = labels.shape[0]
    width = count_blocks * block
    sites = bits.shape[0] * n_sect
    per_dev = left.shape[0]
    pick = per_dev // n_sect
    mine = count_blocks // n_hi

    slabs = lax.all_gather(tensors[0], "sect", axis=0, tiled=False)

    pieces = lax.all_to_all(bits[0].reshape(n_sect, pick), "sect", 0, 0, tiled=False)
    row_bits = jnp.transpose(pieces).astype(left.dtype)

    rows = lax.dynamic_slice_in_dim(left, sect * pick, pick, 0)
    ordered = charge_order(labels, rows, block).reshape(pick, n_hi, mine * block)
    tagged = jnp.broadcast_to(row_bits[:, None, :], (pick, n_hi, sites))
    spread = lax.all_to_all(jnp.concatenate([ordered, tagged], axis=2), "bhi", 1, 1, tiled=False)
    count_rows = n_hi * pick
    spread = jnp.transpose(spread, (1, 0, 2)).reshape(count_rows, mine * block + sites)
    state = spread[:, : mine * block].reshape(count_rows, mine, block).astype(jnp.float32)
    carried_bits = jnp.transpose(spread[:, mine * block :])

    total = jnp.zeros((count_rows,), jnp.float32)
    shift = [(q, (q + 1) % n_hi) for q in range(n_hi)]
    probs = []
    logs = []
    batches = [[0]] + [list(range(k, min(k + 2, sites))) for k in range(1, sites, 2)]
    gathered = {}
    first_slab, state = lax.optimization_barrier((slabs[0:1], state))
    for batch in batches:
        piece = first_slab if batch == [0] else slabs[batch[0] : batch[-1] + 1]
        got = lax.all_gather(piece, "blo", axis=2, tiled=True)
        for index, site in enumerate(batch):
            gathered[site] = got[index]
    for site in range(sites):
        weights = gathered[site]
        image = site_images(state, weights)
        stay = image[0]
        rise = image[1]
        part = jnp.stack([jnp.sum(stay * stay, axis=(1, 2)), jnp.sum(rise * rise, axis=(1, 2))])
        norms = lax.psum(part, "bhi")
        came = lax.ppermute(rise[:, mine - 1], "bhi", shift)
        raised = jnp.concatenate([came[:, None], rise[:, : mine - 1]], axis=1)
        norm_zero = norms[0]
        norm_one = norms[1]
        choose = carried_bits[site] == 1
        chosen_norm = jnp.where(choose, norm_one, norm_zero)
        prob = chosen_norm / (norm_zero + norm_one)
        total = total + jnp.log(prob)
        probs.append(prob)
        logs.append(total)
        if site + 1 < sites:
            chosen = jnp.where(choose[:, None, None], raised, stay)
            state = chosen * lax.rsqrt(chosen_norm / width + 1e-06)[:, None, None]

    result = jnp.stack([jnp.stack(probs), jnp.stack(logs)], axis=1)
    result = lax.dynamic_slice_in_dim(result, bhi * pick, pick, 2)
    back = lax.all_to_all(result, "sect", 0, 0, tiled=False)
    out = jnp.transpose(back, (1, 0, 2)).reshape(2, bits.shape[0], n_sect * pick)
    return (out[0], out[1])


def solution(mesh):
    n_sect, n_blk = mesh.devices.shape
    fine = Mesh(mesh.devices.reshape(n_sect, PARTS, n_blk // PARTS), ("sect", "bhi", "blo"))
    blk = ("bhi", "blo")
    in_specs = (P("sect", blk), P(), P(blk, None), P("sect", None, blk, None, None))
    out_specs = (P("sect", blk), P("sect", blk))
    return jax.shard_map(body, mesh=fine, in_specs=in_specs, out_specs=out_specs, check_vma=False)
```

```python
import jax
import jax.numpy as jnp
from jax import lax
from jax.sharding import Mesh
from jax.sharding import PartitionSpec as P

PARTS = 16


def charge_order(labels, rows, block):
    count_blocks = labels.shape[0]
    blocks = rows.reshape(rows.shape[0], count_blocks, block)
    index = jnp.arange(count_blocks, dtype=jnp.int32)
    pick = (labels[None, :] == index[:, None]).astype(blocks.dtype)
    ordered = jnp.einsum("ci,rik->rck", pick, blocks, preferred_element_type=jnp.float32)
    return ordered.astype(blocks.dtype)


def site_images(state, weights):
    count_rows = state.shape[0]
    rounded = lax.reduce_precision(state, exponent_bits=8, mantissa_bits=7)
    high = rounded.astype(jnp.bfloat16)
    low = (state - rounded).astype(jnp.bfloat16)
    parts = jnp.concatenate([high, low], axis=0)
    both = jnp.einsum("rck,bckl->brcl", parts, weights, preferred_element_type=jnp.float32)
    return both[:, :count_rows] + both[:, count_rows:]


def body(bits, labels, left, tensors):
    sect = lax.axis_index("sect")
    bhi = lax.axis_index("bhi")
    n_sect = lax.axis_size("sect")
    n_hi = lax.axis_size("bhi")
    n_lo = lax.axis_size("blo")
    block = tensors.shape[-1]
    count_blocks = labels.shape[0]
    width = count_blocks * block
    sites = bits.shape[0] * n_sect
    per_dev = left.shape[0]
    pick = per_dev // n_sect
    mine = count_blocks // n_hi

    slabs = lax.all_gather(tensors[0], "sect", axis=0, tiled=False)

    pieces = lax.all_to_all(bits[0].reshape(n_sect, pick), "sect", 0, 0, tiled=False)
    row_bits = jnp.transpose(pieces).astype(left.dtype)

    rows = lax.dynamic_slice_in_dim(left, sect * pick, pick, 0)
    ordered = charge_order(labels, rows, block).reshape(pick, n_lo, n_hi, mine // n_lo, block)
    ordered = jnp.transpose(ordered, (0, 2, 1, 3, 4)).reshape(pick, n_hi, mine * block)
    tagged = jnp.broadcast_to(row_bits[:, None, :], (pick, n_hi, sites))
    spread = lax.all_to_all(jnp.concatenate([ordered, tagged], axis=2), "bhi", 1, 1, tiled=False)
    count_rows = n_hi * pick
    spread = jnp.transpose(spread, (1, 0, 2)).reshape(count_rows, mine * block + sites)
    state = spread[:, : mine * block].reshape(count_rows, mine, block).astype(jnp.float32)
    carried_bits = jnp.transpose(spread[:, mine * block :])

    total = jnp.zeros((count_rows,), jnp.float32)
    shift = [(q, (q + 1) % n_hi) for q in range(n_hi)]
    probs = []
    logs = []
    batches = [[0]] + [list(range(k, min(k + 2, sites))) for k in range(1, sites, 2)]
    gathered = {}
    first_slab, state = lax.optimization_barrier((slabs[0:1], state))
    for batch in batches:
        piece = first_slab if batch == [0] else slabs[batch[0] : batch[-1] + 1]
        got = lax.all_gather(piece, "blo", axis=2, tiled=True)
        for index, site in enumerate(batch):
            gathered[site] = got[index]
    for site in range(sites):
        weights = gathered[site]
        image = site_images(state, weights)
        stay = image[0]
        rise = image[1]
        part = jnp.stack([jnp.sum(stay * stay, axis=(1, 2)), jnp.sum(rise * rise, axis=(1, 2))])
        norms = lax.psum(part, "bhi")
        rise4 = rise.reshape(count_rows, n_lo, mine // n_lo, block)
        send = rise4[:, :, mine // n_lo - 1]
        send = jnp.where(bhi == n_hi - 1, jnp.roll(send, 1, axis=1), send)
        came = lax.ppermute(send, "bhi", shift)
        raised = jnp.stack([came, rise4[:, :, 0]], axis=2).reshape(count_rows, mine, block)
        norm_zero = norms[0]
        norm_one = norms[1]
        choose = carried_bits[site] == 1
        chosen_norm = jnp.where(choose, norm_one, norm_zero)
        prob = chosen_norm / (norm_zero + norm_one)
        total = total + jnp.log(prob)
        probs.append(prob)
        logs.append(total)
        if site + 1 < sites:
            chosen = jnp.where(choose[:, None, None], raised, stay)
            state = chosen * lax.rsqrt(chosen_norm / width + 1e-06)[:, None, None]

    result = jnp.stack([jnp.stack(probs), jnp.stack(logs)], axis=1)
    result = lax.dynamic_slice_in_dim(result, bhi * pick, pick, 2)
    back = lax.all_to_all(result, "sect", 0, 0, tiled=False)
    out = jnp.transpose(back, (1, 0, 2)).reshape(2, bits.shape[0], n_sect * pick)
    return (out[0], out[1])


def solution(mesh):
    n_sect, n_blk = mesh.devices.shape
    fine = Mesh(mesh.devices.reshape(n_sect, n_blk // PARTS, PARTS), ("sect", "blo", "bhi"))
    blk = ("blo", "bhi")
    in_specs = (P("sect", blk), P(), P(blk, None), P("sect", None, blk, None, None))
    out_specs = (P("sect", blk), P("sect", blk))
    return jax.shard_map(body, mesh=fine, in_specs=in_specs, out_specs=out_specs, check_vma=False)
```

```python
import jax
import jax.numpy as jnp
from jax import lax
from jax.sharding import Mesh
from jax.sharding import PartitionSpec as P

PARTS = 8
SECT = ("sx", "sy")


def charge_order(labels, rows, block):
    count_blocks = labels.shape[0]
    blocks = rows.reshape(rows.shape[0], count_blocks, block)
    index = jnp.arange(count_blocks, dtype=jnp.int32)
    pick = (labels[None, :] == index[:, None]).astype(blocks.dtype)
    ordered = jnp.einsum("ci,rik->rck", pick, blocks, preferred_element_type=jnp.float32)
    return ordered.astype(blocks.dtype)


def site_images(state, weights):
    count_rows = state.shape[0]
    rounded = lax.reduce_precision(state, exponent_bits=8, mantissa_bits=7)
    high = rounded.astype(jnp.bfloat16)
    low = (state - rounded).astype(jnp.bfloat16)
    parts = jnp.concatenate([high, low], axis=0)
    both = jnp.einsum("rck,bckl->brcl", parts, weights, preferred_element_type=jnp.float32)
    return both[:, :count_rows] + both[:, count_rows:]


def body(bits, labels, left, tensors):
    sect = lax.axis_index(SECT)
    bhi = lax.axis_index("bhi")
    n_sect = lax.axis_size("sx") * lax.axis_size("sy")
    n_hi = lax.axis_size("bhi")
    n_lo = lax.axis_size("blo")
    block = tensors.shape[-1]
    count_blocks = labels.shape[0]
    width = count_blocks * block
    sites = bits.shape[0] * n_sect
    per_dev = left.shape[0]
    pick = per_dev // n_sect
    mine = count_blocks // n_hi

    slabs = lax.all_gather(tensors[0], "sy", axis=0, tiled=False)
    slabs = lax.all_gather(slabs, "sx", axis=0, tiled=True)

    pieces = lax.all_to_all(bits[0].reshape(n_sect, pick), SECT, 0, 0, tiled=False)
    row_bits = jnp.transpose(pieces).astype(left.dtype)

    rows = lax.dynamic_slice_in_dim(left, sect * pick, pick, 0)
    ordered = charge_order(labels, rows, block).reshape(pick, n_hi, mine * block)
    tagged = jnp.broadcast_to(row_bits[:, None, :], (pick, n_hi, sites))
    spread = lax.all_to_all(jnp.concatenate([ordered, tagged], axis=2), "bhi", 1, 1, tiled=False)
    count_rows = n_hi * pick
    spread = jnp.transpose(spread, (1, 0, 2)).reshape(count_rows, mine * block + sites)
    state = spread[:, : mine * block].reshape(count_rows, mine, block).astype(jnp.float32)
    carried_bits = jnp.transpose(spread[:, mine * block :])

    total = jnp.zeros((count_rows,), jnp.float32)
    shift = [(q, (q + 1) % n_hi) for q in range(n_hi)]
    probs = []
    logs = []
    batches = [[0]] + [list(range(k, min(k + 2, sites))) for k in range(1, sites, 2)]
    gathered = {}
    first_slab, state = lax.optimization_barrier((slabs[0:1], state))
    for batch in batches:
        piece = first_slab if batch == [0] else slabs[batch[0] : batch[-1] + 1]
        got = lax.all_gather(piece, "blo", axis=2, tiled=True)
        for index, site in enumerate(batch):
            gathered[site] = got[index]
    for site in range(sites):
        weights = gathered[site]
        image = site_images(state, weights)
        stay = image[0]
        rise = image[1]
        part = jnp.stack([jnp.sum(stay * stay, axis=(1, 2)), jnp.sum(rise * rise, axis=(1, 2))])
        norms = lax.psum(part, "bhi")
        came = lax.ppermute(rise[:, mine - 1], "bhi", shift)
        raised = jnp.concatenate([came[:, None], rise[:, : mine - 1]], axis=1)
        norm_zero = norms[0]
        norm_one = norms[1]
        choose = carried_bits[site] == 1
        chosen_norm = jnp.where(choose, norm_one, norm_zero)
        prob = chosen_norm / (norm_zero + norm_one)
        total = total + jnp.log(prob)
        probs.append(prob)
        logs.append(total)
        if site + 1 < sites:
            chosen = jnp.where(choose[:, None, None], raised, stay)
            state = chosen * lax.rsqrt(chosen_norm / width + 1e-06)[:, None, None]

    result = jnp.stack([jnp.stack(probs), jnp.stack(logs)], axis=1)
    result = lax.dynamic_slice_in_dim(result, bhi * pick, pick, 2)
    back = lax.all_to_all(result, SECT, 0, 0, tiled=False)
    out = jnp.transpose(back, (1, 0, 2)).reshape(2, bits.shape[0], n_sect * pick)
    return (out[0], out[1])


def solution(mesh):
    n_sect, n_blk = mesh.devices.shape
    n_x = n_sect // 2
    fine = Mesh(mesh.devices.reshape(n_x, 2, PARTS, n_blk // PARTS), ("sx", "sy", "bhi", "blo"))
    blk = ("bhi", "blo")
    in_specs = (P(SECT, blk), P(), P(blk, None), P(SECT, None, blk, None, None))
    out_specs = (P(SECT, blk), P(SECT, blk))
    return jax.shard_map(body, mesh=fine, in_specs=in_specs, out_specs=out_specs, check_vma=False)
```

```python
import jax
import jax.numpy as jnp
from jax import lax
from jax.sharding import Mesh
from jax.sharding import PartitionSpec as P

PARTS = 8
SECT = ("sx", "sy")


def charge_order(labels, rows, block):
    count_blocks = labels.shape[0]
    blocks = rows.reshape(rows.shape[0], count_blocks, block)
    index = jnp.arange(count_blocks, dtype=jnp.int32)
    pick = (labels[None, :] == index[:, None]).astype(blocks.dtype)
    ordered = jnp.einsum("ci,rik->rck", pick, blocks, preferred_element_type=jnp.float32)
    return ordered.astype(blocks.dtype)


def site_images(state, weights):
    count_rows = state.shape[0]
    rounded = lax.reduce_precision(state, exponent_bits=8, mantissa_bits=7)
    high = rounded.astype(jnp.bfloat16)
    low = (state - rounded).astype(jnp.bfloat16)
    parts = jnp.concatenate([high, low], axis=0)
    both = jnp.einsum("rck,bckl->brcl", parts, weights, preferred_element_type=jnp.float32)
    return both[:, :count_rows] + both[:, count_rows:]


def body(bits, labels, left, tensors):
    sect = lax.axis_index(SECT)
    bhi = lax.axis_index("bhi")
    n_sect = lax.axis_size("sx") * lax.axis_size("sy")
    n_hi = lax.axis_size("bhi")
    n_lo = lax.axis_size("blo")
    block = tensors.shape[-1]
    count_blocks = labels.shape[0]
    width = count_blocks * block
    sites = bits.shape[0] * n_sect
    per_dev = left.shape[0]
    pick = per_dev // n_sect
    mine = count_blocks // n_hi

    slabs = lax.all_gather(tensors[0], "sy", axis=0, tiled=False)
    slabs = lax.all_gather(slabs, "sx", axis=0, tiled=True)

    pieces = lax.all_to_all(bits[0].reshape(n_sect, pick), SECT, 0, 0, tiled=False)
    row_bits = jnp.transpose(pieces).astype(left.dtype)

    rows = lax.dynamic_slice_in_dim(left, sect * pick, pick, 0)
    ordered = charge_order(labels, rows, block).reshape(pick, n_hi, mine * block)
    tagged = jnp.broadcast_to(row_bits[:, None, :], (pick, n_hi, sites))
    spread = lax.all_to_all(jnp.concatenate([ordered, tagged], axis=2), "bhi", 1, 1, tiled=False)
    count_rows = n_hi * pick
    spread = jnp.transpose(spread, (1, 0, 2)).reshape(count_rows, mine * block + sites)
    state = spread[:, : mine * block].reshape(count_rows, mine, block).astype(jnp.float32)
    carried_bits = jnp.transpose(spread[:, mine * block :])

    total = jnp.zeros((count_rows,), jnp.float32)
    shift = [(q, (q + 1) % n_hi) for q in range(n_hi)]
    probs = []
    logs = []
    batches = [[0]] + [list(range(k, min(k + 2, sites))) for k in range(1, sites, 2)]
    gathered = {}
    for batch in batches:
        got = lax.all_gather(slabs[batch[0] : batch[-1] + 1], "blo", axis=2, tiled=True)
        for index, site in enumerate(batch):
            gathered[site] = got[index]
    for site in range(sites):
        weights = gathered[site]
        image = site_images(state, weights)
        stay = image[0]
        rise = image[1]
        part = jnp.stack([jnp.sum(stay * stay, axis=(1, 2)), jnp.sum(rise * rise, axis=(1, 2))])
        norms = lax.psum(part, "bhi")
        came = lax.ppermute(rise[:, mine - 1], "bhi", shift)
        raised = jnp.concatenate([came[:, None], rise[:, : mine - 1]], axis=1)
        norm_zero = norms[0]
        norm_one = norms[1]
        choose = carried_bits[site] == 1
        chosen_norm = jnp.where(choose, norm_one, norm_zero)
        prob = chosen_norm / (norm_zero + norm_one)
        total = total + jnp.log(prob)
        probs.append(prob)
        logs.append(total)
        if site + 1 < sites:
            chosen = jnp.where(choose[:, None, None], raised, stay)
            state = chosen * lax.rsqrt(chosen_norm / width + 1e-06)[:, None, None]

    result = jnp.stack([jnp.stack(probs), jnp.stack(logs)], axis=1)
    result = lax.dynamic_slice_in_dim(result, bhi * pick, pick, 2)
    back = lax.all_to_all(result, SECT, 0, 0, tiled=False)
    out = jnp.transpose(back, (1, 0, 2)).reshape(2, bits.shape[0], n_sect * pick)
    return (out[0], out[1])


def solution(mesh):
    n_sect, n_blk = mesh.devices.shape
    n_x = n_sect // 2
    fine = Mesh(mesh.devices.reshape(n_x, 2, PARTS, n_blk // PARTS), ("sx", "sy", "bhi", "blo"))
    blk = ("bhi", "blo")
    in_specs = (P(SECT, blk), P(), P(blk, None), P(SECT, None, blk, None, None))
    out_specs = (P(SECT, blk), P(SECT, blk))
    return jax.shard_map(body, mesh=fine, in_specs=in_specs, out_specs=out_specs, check_vma=False)
```

```python
import jax
import jax.numpy as jnp
from jax import lax
from jax.sharding import Mesh
from jax.sharding import PartitionSpec as P

PARTS = 8
SECT = ("sx", "sy")
BHI = ("bh1", "bh2")


def charge_order(labels, rows, block):
    count_blocks = labels.shape[0]
    blocks = rows.reshape(rows.shape[0], count_blocks, block)
    index = jnp.arange(count_blocks, dtype=jnp.int32)
    pick = (labels[None, :] == index[:, None]).astype(blocks.dtype)
    ordered = jnp.einsum("ci,rik->rck", pick, blocks, preferred_element_type=jnp.float32)
    return ordered.astype(blocks.dtype)


def site_images(state, weights):
    count_rows = state.shape[0]
    rounded = lax.reduce_precision(state, exponent_bits=8, mantissa_bits=7)
    high = rounded.astype(jnp.bfloat16)
    low = (state - rounded).astype(jnp.bfloat16)
    parts = jnp.concatenate([high, low], axis=0)
    both = jnp.einsum("rck,bckl->brcl", parts, weights, preferred_element_type=jnp.float32)
    return both[:, :count_rows] + both[:, count_rows:]


def body(bits, labels, left, tensors):
    sect = lax.axis_index(SECT)
    bhi = lax.axis_index(BHI)
    n_sect = lax.axis_size("sx") * lax.axis_size("sy")
    n_hi = lax.axis_size("bh1") * lax.axis_size("bh2")
    n_lo = lax.axis_size("blo")
    block = tensors.shape[-1]
    count_blocks = labels.shape[0]
    width = count_blocks * block
    sites = bits.shape[0] * n_sect
    per_dev = left.shape[0]
    pick = per_dev // n_sect
    mine = count_blocks // n_hi

    slabs = lax.all_gather(tensors[0], "sy", axis=0, tiled=False)
    slabs = lax.all_gather(slabs, "sx", axis=0, tiled=True)

    pieces = lax.all_to_all(bits[0].reshape(n_sect, pick), SECT, 0, 0, tiled=False)
    row_bits = jnp.transpose(pieces).astype(left.dtype)

    rows = lax.dynamic_slice_in_dim(left, sect * pick, pick, 0)
    ordered = charge_order(labels, rows, block).reshape(pick, n_hi, mine * block)
    tagged = jnp.broadcast_to(row_bits[:, None, :], (pick, n_hi, sites))
    spread = lax.all_to_all(jnp.concatenate([ordered, tagged], axis=2), BHI, 1, 1, tiled=False)
    count_rows = n_hi * pick
    spread = jnp.transpose(spread, (1, 0, 2)).reshape(count_rows, mine * block + sites)
    state = spread[:, : mine * block].reshape(count_rows, mine, block).astype(jnp.float32)
    carried_bits = jnp.transpose(spread[:, mine * block :])

    total = jnp.zeros((count_rows,), jnp.float32)
    shift = [(q, (q + 1) % n_hi) for q in range(n_hi)]
    probs = []
    logs = []
    batches = [[0]] + [list(range(k, min(k + 2, sites))) for k in range(1, sites, 2)]
    gathered = {}
    first_slab, state = lax.optimization_barrier((slabs[0:1], state))
    for batch in batches:
        piece = first_slab if batch == [0] else slabs[batch[0] : batch[-1] + 1]
        got = lax.all_gather(piece, "blo", axis=2, tiled=True)
        for index, site in enumerate(batch):
            gathered[site] = got[index]
    for site in range(sites):
        weights = gathered[site]
        image = site_images(state, weights)
        stay = image[0]
        rise = image[1]
        part = jnp.stack([jnp.sum(stay * stay, axis=(1, 2)), jnp.sum(rise * rise, axis=(1, 2))])
        norms = lax.optimization_barrier(lax.psum(part, "bh2"))
        norms = lax.psum(norms, "bh1")
        came = lax.ppermute(rise[:, mine - 1], BHI, shift)
        raised = jnp.concatenate([came[:, None], rise[:, : mine - 1]], axis=1)
        norm_zero = norms[0]
        norm_one = norms[1]
        choose = carried_bits[site] == 1
        chosen_norm = jnp.where(choose, norm_one, norm_zero)
        prob = chosen_norm / (norm_zero + norm_one)
        total = total + jnp.log(prob)
        probs.append(prob)
        logs.append(total)
        if site + 1 < sites:
            chosen = jnp.where(choose[:, None, None], raised, stay)
            state = chosen * lax.rsqrt(chosen_norm / width + 1e-06)[:, None, None]

    result = jnp.stack([jnp.stack(probs), jnp.stack(logs)], axis=1)
    result = lax.dynamic_slice_in_dim(result, bhi * pick, pick, 2)
    back = lax.all_to_all(result, SECT, 0, 0, tiled=False)
    out = jnp.transpose(back, (1, 0, 2)).reshape(2, bits.shape[0], n_sect * pick)
    return (out[0], out[1])


def solution(mesh):
    n_sect, n_blk = mesh.devices.shape
    n_x = n_sect // 2
    grid = mesh.devices.reshape(n_x, 2, PARTS // 2, 2, n_blk // PARTS)
    fine = Mesh(grid, ("sx", "sy", "bh1", "bh2", "blo"))
    blk = ("bh1", "bh2", "blo")
    in_specs = (P(SECT, blk), P(), P(blk, None), P(SECT, None, blk, None, None))
    out_specs = (P(SECT, blk), P(SECT, blk))
    return jax.shard_map(body, mesh=fine, in_specs=in_specs, out_specs=out_specs, check_vma=False)
```

```python
import jax
import jax.numpy as jnp
from jax import lax
from jax.sharding import Mesh
from jax.sharding import PartitionSpec as P

PARTS = 8
SECT = ("sx", "sy")
BHI = ("bh1", "bh2", "bh3")


def charge_order(labels, rows, block):
    count_blocks = labels.shape[0]
    blocks = rows.reshape(rows.shape[0], count_blocks, block)
    index = jnp.arange(count_blocks, dtype=jnp.int32)
    pick = (labels[None, :] == index[:, None]).astype(blocks.dtype)
    ordered = jnp.einsum("ci,rik->rck", pick, blocks, preferred_element_type=jnp.float32)
    return ordered.astype(blocks.dtype)


def site_images(state, weights):
    count_rows = state.shape[0]
    rounded = lax.reduce_precision(state, exponent_bits=8, mantissa_bits=7)
    high = rounded.astype(jnp.bfloat16)
    low = (state - rounded).astype(jnp.bfloat16)
    parts = jnp.concatenate([high, low], axis=0)
    both = jnp.einsum("rck,bckl->brcl", parts, weights, preferred_element_type=jnp.float32)
    return both[:, :count_rows] + both[:, count_rows:]


def body(bits, labels, left, tensors):
    sect = lax.axis_index(SECT)
    bhi = lax.axis_index(BHI)
    n_sect = lax.axis_size("sx") * lax.axis_size("sy")
    n_hi = lax.axis_size("bh1") * lax.axis_size("bh2") * lax.axis_size("bh3")
    n_lo = lax.axis_size("blo")
    block = tensors.shape[-1]
    count_blocks = labels.shape[0]
    width = count_blocks * block
    sites = bits.shape[0] * n_sect
    per_dev = left.shape[0]
    pick = per_dev // n_sect
    mine = count_blocks // n_hi

    slabs = lax.all_gather(tensors[0], "sy", axis=0, tiled=False)
    slabs = lax.all_gather(slabs, "sx", axis=0, tiled=True)

    pieces = lax.all_to_all(bits[0].reshape(n_sect, pick), SECT, 0, 0, tiled=False)
    row_bits = jnp.transpose(pieces).astype(left.dtype)

    rows = lax.dynamic_slice_in_dim(left, sect * pick, pick, 0)
    ordered = charge_order(labels, rows, block).reshape(pick, n_hi, mine * block)
    tagged = jnp.broadcast_to(row_bits[:, None, :], (pick, n_hi, sites))
    spread = lax.all_to_all(jnp.concatenate([ordered, tagged], axis=2), BHI, 1, 1, tiled=False)
    count_rows = n_hi * pick
    spread = jnp.transpose(spread, (1, 0, 2)).reshape(count_rows, mine * block + sites)
    state = spread[:, : mine * block].reshape(count_rows, mine, block).astype(jnp.float32)
    carried_bits = jnp.transpose(spread[:, mine * block :])

    total = jnp.zeros((count_rows,), jnp.float32)
    shift = [(q, (q + 1) % n_hi) for q in range(n_hi)]
    probs = []
    logs = []
    batches = [[0]] + [list(range(k, min(k + 2, sites))) for k in range(1, sites, 2)]
    gathered = {}
    first_slab, state = lax.optimization_barrier((slabs[0:1], state))
    for batch in batches:
        piece = first_slab if batch == [0] else slabs[batch[0] : batch[-1] + 1]
        got = lax.all_gather(piece, "blo", axis=2, tiled=True)
        for index, site in enumerate(batch):
            gathered[site] = got[index]
    for site in range(sites):
        weights = gathered[site]
        image = site_images(state, weights)
        stay = image[0]
        rise = image[1]
        part = jnp.stack([jnp.sum(stay * stay, axis=(1, 2)), jnp.sum(rise * rise, axis=(1, 2))])
        norms = lax.optimization_barrier(lax.psum(part, "bh3"))
        norms = lax.optimization_barrier(lax.psum(norms, "bh2"))
        norms = lax.psum(norms, "bh1")
        came = lax.ppermute(rise[:, mine - 1], BHI, shift)
        raised = jnp.concatenate([came[:, None], rise[:, : mine - 1]], axis=1)
        norm_zero = norms[0]
        norm_one = norms[1]
        choose = carried_bits[site] == 1
        chosen_norm = jnp.where(choose, norm_one, norm_zero)
        prob = chosen_norm / (norm_zero + norm_one)
        total = total + jnp.log(prob)
        probs.append(prob)
        logs.append(total)
        if site + 1 < sites:
            chosen = jnp.where(choose[:, None, None], raised, stay)
            state = chosen * lax.rsqrt(chosen_norm / width + 1e-06)[:, None, None]

    result = jnp.stack([jnp.stack(probs), jnp.stack(logs)], axis=1)
    result = lax.dynamic_slice_in_dim(result, bhi * pick, pick, 2)
    back = lax.all_to_all(result, SECT, 0, 0, tiled=False)
    out = jnp.transpose(back, (1, 0, 2)).reshape(2, bits.shape[0], n_sect * pick)
    return (out[0], out[1])


def solution(mesh):
    n_sect, n_blk = mesh.devices.shape
    n_x = n_sect // 2
    grid = mesh.devices.reshape(n_x, 2, PARTS // 4, 2, 2, n_blk // PARTS)
    fine = Mesh(grid, ("sx", "sy", "bh1", "bh2", "bh3", "blo"))
    blk = ("bh1", "bh2", "bh3", "blo")
    in_specs = (P(SECT, blk), P(), P(blk, None), P(SECT, None, blk, None, None))
    out_specs = (P(SECT, blk), P(SECT, blk))
    return jax.shard_map(body, mesh=fine, in_specs=in_specs, out_specs=out_specs, check_vma=False)
```

```python
import jax
import jax.numpy as jnp
from jax import lax
from jax.sharding import Mesh
from jax.sharding import PartitionSpec as P

PARTS = 8
SECT = ("sx", "sy")
GATHER = ("g1", "g2")


def charge_order(labels, rows, block):
    count_blocks = labels.shape[0]
    blocks = rows.reshape(rows.shape[0], count_blocks, block)
    index = jnp.arange(count_blocks, dtype=jnp.int32)
    pick = (labels[None, :] == index[:, None]).astype(blocks.dtype)
    ordered = jnp.einsum("ci,rik->rck", pick, blocks, preferred_element_type=jnp.float32)
    return ordered.astype(blocks.dtype)


def site_images(state, weights):
    count_rows = state.shape[0]
    rounded = lax.reduce_precision(state, exponent_bits=8, mantissa_bits=7)
    high = rounded.astype(jnp.bfloat16)
    low = (state - rounded).astype(jnp.bfloat16)
    parts = jnp.concatenate([high, low], axis=0)
    both = jnp.einsum("rck,bckl->brcl", parts, weights, preferred_element_type=jnp.float32)
    return both[:, :count_rows] + both[:, count_rows:]


def body(bits, labels, left, tensors):
    sect = lax.axis_index(SECT)
    bhi = lax.axis_index("bhi")
    n_sect = lax.axis_size("sx") * lax.axis_size("sy")
    n_hi = lax.axis_size("bhi")
    n_lo = lax.axis_size("g1")
    block = tensors.shape[-1]
    count_blocks = labels.shape[0]
    width = count_blocks * block
    sites = bits.shape[0] * n_sect
    per_dev = left.shape[0]
    pick = per_dev // n_sect
    mine = count_blocks // n_hi

    slabs = lax.all_gather(tensors[0], "sy", axis=0, tiled=False)
    slabs = lax.all_gather(slabs, "sx", axis=0, tiled=True)

    pieces = lax.all_to_all(bits[0].reshape(n_sect, pick), SECT, 0, 0, tiled=False)
    row_bits = jnp.transpose(pieces).astype(left.dtype)

    rows = lax.dynamic_slice_in_dim(left, sect * pick, pick, 0)
    ordered = charge_order(labels, rows, block).reshape(pick, n_lo, n_hi, mine // n_lo, block)
    ordered = jnp.transpose(ordered, (0, 2, 1, 3, 4)).reshape(pick, n_hi, mine * block)
    tagged = jnp.broadcast_to(row_bits[:, None, :], (pick, n_hi, sites))
    spread = lax.all_to_all(jnp.concatenate([ordered, tagged], axis=2), "bhi", 1, 1, tiled=False)
    count_rows = n_hi * pick
    spread = jnp.transpose(spread, (1, 0, 2)).reshape(count_rows, mine * block + sites)
    state = spread[:, : mine * block].reshape(count_rows, mine, block).astype(jnp.float32)
    carried_bits = jnp.transpose(spread[:, mine * block :])

    total = jnp.zeros((count_rows,), jnp.float32)
    shift = [(q, (q + 1) % n_hi) for q in range(n_hi)]
    probs = []
    logs = []
    batches = [[0]] + [list(range(k, min(k + 2, sites))) for k in range(1, sites, 2)]
    gathered = {}
    first_slab, state = lax.optimization_barrier((slabs[0:1], state))
    for batch in batches:
        piece = first_slab if batch == [0] else slabs[batch[0] : batch[-1] + 1]
        got = lax.all_gather(piece, GATHER, axis=2, tiled=True)
        for index, site in enumerate(batch):
            gathered[site] = got[index]
    for site in range(sites):
        weights = gathered[site]
        image = site_images(state, weights)
        stay = image[0]
        rise = image[1]
        part = jnp.stack([jnp.sum(stay * stay, axis=(1, 2)), jnp.sum(rise * rise, axis=(1, 2))])
        norms = lax.psum(part, "bhi")
        rise4 = rise.reshape(count_rows, n_lo, mine // n_lo, block)
        send = rise4[:, :, mine // n_lo - 1]
        send = jnp.where(bhi == n_hi - 1, jnp.roll(send, 1, axis=1), send)
        came = lax.ppermute(send, "bhi", shift)
        raised = jnp.concatenate([came[:, :, None], rise4[:, :, : mine // n_lo - 1]], axis=2)
        raised = raised.reshape(count_rows, mine, block)
        norm_zero = norms[0]
        norm_one = norms[1]
        choose = carried_bits[site] == 1
        chosen_norm = jnp.where(choose, norm_one, norm_zero)
        prob = chosen_norm / (norm_zero + norm_one)
        total = total + jnp.log(prob)
        probs.append(prob)
        logs.append(total)
        if site + 1 < sites:
            chosen = jnp.where(choose[:, None, None], raised, stay)
            state = chosen * lax.rsqrt(chosen_norm / width + 1e-06)[:, None, None]

    result = jnp.stack([jnp.stack(probs), jnp.stack(logs)], axis=1)
    result = lax.dynamic_slice_in_dim(result, bhi * pick, pick, 2)
    back = lax.all_to_all(result, SECT, 0, 0, tiled=False)
    out = jnp.transpose(back, (1, 0, 2)).reshape(2, bits.shape[0], n_sect * pick)
    return (out[0], out[1])


def solution(mesh):
    n_sect, n_blk = mesh.devices.shape
    n_x = n_sect // 2
    grid = mesh.devices.reshape(n_x, 2, 2, PARTS, n_blk // (2 * PARTS))
    fine = Mesh(grid, ("sx", "sy", "g1", "bhi", "g2"))
    blk = ("g1", "bhi", "g2")
    in_specs = (P(SECT, blk), P(), P(blk, None), P(SECT, None, blk, None, None))
    out_specs = (P(SECT, blk), P(SECT, blk))
    return jax.shard_map(body, mesh=fine, in_specs=in_specs, out_specs=out_specs, check_vma=False)
```

```python
import jax
import jax.numpy as jnp
from jax import lax
from jax.sharding import Mesh
from jax.sharding import PartitionSpec as P

PARTS = 8
SECT = ("sx", "sy")


def charge_order(labels, rows, block):
    count_blocks = labels.shape[0]
    blocks = rows.reshape(rows.shape[0], count_blocks, block)
    index = jnp.arange(count_blocks, dtype=jnp.int32)
    pick = (labels[None, :] == index[:, None]).astype(blocks.dtype)
    ordered = jnp.einsum("ci,rik->rck", pick, blocks, preferred_element_type=jnp.float32)
    return ordered.astype(blocks.dtype)


def site_images(state, weights):
    count_rows = state.shape[0]
    rounded = lax.reduce_precision(state, exponent_bits=8, mantissa_bits=7)
    high = rounded.astype(jnp.bfloat16)
    low = (state - rounded).astype(jnp.bfloat16)
    parts = jnp.concatenate([high, low], axis=0)
    both = jnp.einsum("rck,bckl->brcl", parts, weights, preferred_element_type=jnp.float32)
    return both[:, :count_rows] + both[:, count_rows:]


def body(bits, labels, left, tensors):
    sect = lax.axis_index(SECT)
    bhi = lax.axis_index("bhi")
    n_sect = lax.axis_size("sx") * lax.axis_size("sy")
    n_hi = lax.axis_size("bhi")
    n_lo = lax.axis_size("blo")
    block = tensors.shape[-1]
    count_blocks = labels.shape[0]
    width = count_blocks * block
    sites = bits.shape[0] * n_sect
    per_dev = left.shape[0]
    pick = per_dev // n_sect
    mine = count_blocks // n_hi

    slabs = lax.all_gather(tensors[0], "sy", axis=0, tiled=False)
    slabs = lax.all_gather(slabs, "sx", axis=0, tiled=True)

    pieces = lax.all_to_all(bits[0].reshape(n_sect, pick), SECT, 0, 0, tiled=False)
    row_bits = jnp.transpose(pieces).astype(left.dtype)

    rows = lax.dynamic_slice_in_dim(left, sect * pick, pick, 0)
    ordered = charge_order(labels, rows, block).reshape(pick, width)
    tagged = jnp.concatenate([ordered, row_bits], axis=1)
    spread = lax.all_gather(tagged, "bhi", axis=0, tiled=False)
    count_rows = n_hi * pick
    spread = spread.reshape(count_rows, width + sites)
    state = lax.dynamic_slice_in_dim(spread, bhi * mine * block, mine * block, 1)
    state = state.reshape(count_rows, mine, block).astype(jnp.float32)
    carried_bits = jnp.transpose(spread[:, width:])

    total = jnp.zeros((count_rows,), jnp.float32)
    shift = [(q, (q + 1) % n_hi) for q in range(n_hi)]
    probs = []
    logs = []
    batches = [[0]] + [list(range(k, min(k + 2, sites))) for k in range(1, sites, 2)]
    gathered = {}
    for batch in batches:
        got = lax.all_gather(slabs[batch[0] : batch[-1] + 1], "blo", axis=2, tiled=True)
        for index, site in enumerate(batch):
            gathered[site] = got[index]
    for site in range(sites):
        weights = gathered[site]
        image = site_images(state, weights)
        stay = image[0]
        rise = image[1]
        part = jnp.stack([jnp.sum(stay * stay, axis=(1, 2)), jnp.sum(rise * rise, axis=(1, 2))])
        norms = lax.psum(part, "bhi")
        came = lax.ppermute(rise[:, mine - 1], "bhi", shift)
        raised = jnp.concatenate([came[:, None], rise[:, : mine - 1]], axis=1)
        norm_zero = norms[0]
        norm_one = norms[1]
        choose = carried_bits[site] == 1
        chosen_norm = jnp.where(choose, norm_one, norm_zero)
        prob = chosen_norm / (norm_zero + norm_one)
        total = total + jnp.log(prob)
        probs.append(prob)
        logs.append(total)
        if site + 1 < sites:
            chosen = jnp.where(choose[:, None, None], raised, stay)
            state = chosen * lax.rsqrt(chosen_norm / width + 1e-06)[:, None, None]

    result = jnp.stack([jnp.stack(probs), jnp.stack(logs)], axis=1)
    result = lax.dynamic_slice_in_dim(result, bhi * pick, pick, 2)
    back = lax.all_to_all(result, SECT, 0, 0, tiled=False)
    out = jnp.transpose(back, (1, 0, 2)).reshape(2, bits.shape[0], n_sect * pick)
    return (out[0], out[1])


def solution(mesh):
    n_sect, n_blk = mesh.devices.shape
    n_x = n_sect // 2
    fine = Mesh(mesh.devices.reshape(n_x, 2, PARTS, n_blk // PARTS), ("sx", "sy", "bhi", "blo"))
    blk = ("bhi", "blo")
    in_specs = (P(SECT, blk), P(), P(blk, None), P(SECT, None, blk, None, None))
    out_specs = (P(SECT, blk), P(SECT, blk))
    return jax.shard_map(body, mesh=fine, in_specs=in_specs, out_specs=out_specs, check_vma=False)
```

```python
import jax
import jax.numpy as jnp
from jax import lax
from jax.sharding import Mesh
from jax.sharding import PartitionSpec as P

PARTS = 8
SECT = ("sx", "sy")


def charge_order(labels, rows, block):
    count_blocks = labels.shape[0]
    blocks = rows.reshape(rows.shape[0], count_blocks, block)
    index = jnp.arange(count_blocks, dtype=jnp.int32)
    pick = (labels[None, :] == index[:, None]).astype(blocks.dtype)
    ordered = jnp.einsum("ci,rik->rck", pick, blocks, preferred_element_type=jnp.float32)
    return ordered.astype(blocks.dtype)


def site_images(state, weights):
    count_rows = state.shape[0]
    rounded = lax.reduce_precision(state, exponent_bits=8, mantissa_bits=7)
    high = rounded.astype(jnp.bfloat16)
    low = (state - rounded).astype(jnp.bfloat16)
    parts = jnp.concatenate([high, low], axis=0)
    both = jnp.einsum("rck,bckl->brcl", parts, weights, preferred_element_type=jnp.float32)
    return both[:, :count_rows] + both[:, count_rows:]


def body(bits, labels, left, tensors):
    sect = lax.axis_index(SECT)
    bhi = lax.axis_index("bhi")
    n_sect = lax.axis_size("sx") * lax.axis_size("sy")
    n_hi = lax.axis_size("bhi")
    n_lo = lax.axis_size("blo")
    block = tensors.shape[-1]
    count_blocks = labels.shape[0]
    width = count_blocks * block
    sites = bits.shape[0] * n_sect
    per_dev = left.shape[0]
    pick = per_dev // n_sect
    mine = count_blocks // n_hi

    slabs = lax.all_gather(tensors[0], "sy", axis=0, tiled=False)
    slabs = lax.all_gather(slabs, "sx", axis=0, tiled=True)

    rows = lax.dynamic_slice_in_dim(left, sect * pick, pick, 0)
    ordered = charge_order(labels, rows, block).reshape(pick, n_hi, mine * block)
    spread = lax.all_to_all(ordered, "bhi", 1, 1, tiled=False)
    count_rows = n_hi * pick
    state = jnp.transpose(spread, (1, 0, 2)).reshape(count_rows, mine, block).astype(jnp.float32)

    first_slab, state, late_bits = lax.optimization_barrier((slabs[0:1], state, bits))
    pieces = lax.all_to_all(late_bits[0].reshape(n_sect, pick), SECT, 0, 0, tiled=False)
    row_bits = pieces.reshape(1, sites * pick)
    row_bits = jnp.broadcast_to(row_bits, (n_hi, sites * pick))
    carried_bits = lax.all_to_all(row_bits, "bhi", 0, 0, tiled=False).reshape(n_hi, sites, pick)
    carried_bits = jnp.transpose(carried_bits, (1, 0, 2)).reshape(sites, count_rows)

    total = jnp.zeros((count_rows,), jnp.float32)
    shift = [(q, (q + 1) % n_hi) for q in range(n_hi)]
    probs = []
    logs = []
    batches = [[0]] + [list(range(k, min(k + 2, sites))) for k in range(1, sites, 2)]
    gathered = {}
    for batch in batches:
        piece = first_slab if batch == [0] else slabs[batch[0] : batch[-1] + 1]
        got = lax.all_gather(piece, "blo", axis=2, tiled=True)
        for index, site in enumerate(batch):
            gathered[site] = got[index]
    for site in range(sites):
        weights = gathered[site]
        image = site_images(state, weights)
        stay = image[0]
        rise = image[1]
        part = jnp.stack([jnp.sum(stay * stay, axis=(1, 2)), jnp.sum(rise * rise, axis=(1, 2))])
        norms = lax.psum(part, "bhi")
        came = lax.ppermute(rise[:, mine - 1], "bhi", shift)
        raised = jnp.concatenate([came[:, None], rise[:, : mine - 1]], axis=1)
        norm_zero = norms[0]
        norm_one = norms[1]
        choose = carried_bits[site] == 1
        chosen_norm = jnp.where(choose, norm_one, norm_zero)
        prob = chosen_norm / (norm_zero + norm_one)
        total = total + jnp.log(prob)
        probs.append(prob)
        logs.append(total)
        if site + 1 < sites:
            chosen = jnp.where(choose[:, None, None], raised, stay)
            state = chosen * lax.rsqrt(chosen_norm / width + 1e-06)[:, None, None]

    result = jnp.stack([jnp.stack(probs), jnp.stack(logs)], axis=1)
    result = lax.dynamic_slice_in_dim(result, bhi * pick, pick, 2)
    back = lax.all_to_all(result, SECT, 0, 0, tiled=False)
    out = jnp.transpose(back, (1, 0, 2)).reshape(2, bits.shape[0], n_sect * pick)
    return (out[0], out[1])


def solution(mesh):
    n_sect, n_blk = mesh.devices.shape
    n_x = n_sect // 2
    fine = Mesh(mesh.devices.reshape(n_x, 2, PARTS, n_blk // PARTS), ("sx", "sy", "bhi", "blo"))
    blk = ("bhi", "blo")
    in_specs = (P(SECT, blk), P(), P(blk, None), P(SECT, None, blk, None, None))
    out_specs = (P(SECT, blk), P(SECT, blk))
    return jax.shard_map(body, mesh=fine, in_specs=in_specs, out_specs=out_specs, check_vma=False)
```

```python
import jax
import jax.numpy as jnp
from jax import lax
from jax.sharding import Mesh
from jax.sharding import PartitionSpec as P

PARTS = 8
SECT = ("sx", "sy")


def charge_order(labels, rows, block):
    count_blocks = labels.shape[0]
    blocks = rows.reshape(rows.shape[0], count_blocks, block)
    index = jnp.arange(count_blocks, dtype=jnp.int32)
    pick = (labels[None, :] == index[:, None]).astype(blocks.dtype)
    ordered = jnp.einsum("ci,rik->rck", pick, blocks, preferred_element_type=jnp.float32)
    return ordered.astype(blocks.dtype)


def site_images(state, weights):
    count_rows = state.shape[0]
    rounded = lax.reduce_precision(state, exponent_bits=8, mantissa_bits=7)
    high = rounded.astype(jnp.bfloat16)
    low = (state - rounded).astype(jnp.bfloat16)
    parts = jnp.concatenate([high, low], axis=0)
    both = jnp.einsum("rck,bckl->brcl", parts, weights, preferred_element_type=jnp.float32)
    return both[:, :count_rows] + both[:, count_rows:]


def body(bits, labels, left, tensors):
    sect = lax.axis_index(SECT)
    bhi = lax.axis_index("bhi")
    n_sect = lax.axis_size("sx") * lax.axis_size("sy")
    n_hi = lax.axis_size("bhi")
    n_lo = lax.axis_size("blo")
    block = tensors.shape[-1]
    count_blocks = labels.shape[0]
    width = count_blocks * block
    sites = bits.shape[0] * n_sect
    per_dev = left.shape[0]
    pick = per_dev // n_sect
    mine = count_blocks // n_hi

    slabs = lax.all_gather(tensors[0], "sy", axis=0, tiled=False)
    slabs = lax.all_gather(slabs, "sx", axis=0, tiled=True)

    rows = lax.dynamic_slice_in_dim(left, sect * pick, pick, 0)
    ordered = charge_order(labels, rows, block).reshape(pick, n_hi, mine * block)
    spread = lax.all_to_all(ordered, "bhi", 1, 1, tiled=False)
    count_rows = n_hi * pick
    state = jnp.transpose(spread, (1, 0, 2)).reshape(count_rows, mine, block).astype(jnp.float32)

    first_slab, state, late_bits = lax.optimization_barrier((slabs[0:1], state, bits))
    pieces = lax.all_to_all(late_bits[0].reshape(n_sect, pick), SECT, 0, 0, tiled=False)
    row_bits = pieces.reshape(1, sites * pick)
    row_bits = jnp.broadcast_to(row_bits, (n_hi, sites * pick))
    carried_bits = lax.all_to_all(row_bits, "bhi", 0, 0, tiled=False).reshape(n_hi, sites, pick)
    carried_bits = jnp.transpose(carried_bits, (1, 0, 2)).reshape(sites, count_rows)

    total = jnp.zeros((count_rows,), jnp.float32)
    shift = [(q, (q + 1) % n_hi) for q in range(n_hi)]
    probs = []
    logs = []
    batches = [[0]] + [list(range(k, min(k + 2, sites))) for k in range(1, sites, 2)]
    gathered = {}
    for batch in batches:
        piece = first_slab if batch == [0] else slabs[batch[0] : batch[-1] + 1]
        got = lax.all_gather(piece, "blo", axis=2, tiled=True)
        for index, site in enumerate(batch):
            gathered[site] = got[index]
    for site in range(sites):
        weights = gathered[site]
        image = site_images(state, weights)
        stay = image[0]
        rise = image[1]
        part = jnp.stack([jnp.sum(stay * stay, axis=(1, 2)), jnp.sum(rise * rise, axis=(1, 2))])
        norms = lax.psum(part, "bhi")
        came = lax.ppermute(rise[:, mine - 1], "bhi", shift)
        raised = jnp.concatenate([came[:, None], rise[:, : mine - 1]], axis=1)
        norm_zero = norms[0]
        norm_one = norms[1]
        choose = carried_bits[site] == 1
        chosen_norm = jnp.where(choose, norm_one, norm_zero)
        prob = chosen_norm / (norm_zero + norm_one)
        total = total + jnp.log(prob)
        probs.append(prob)
        logs.append(total)
        if site + 1 < sites:
            chosen = jnp.where(choose[:, None, None], raised, stay)
            state = chosen * lax.rsqrt(chosen_norm / width + 1e-06)[:, None, None]

    result = jnp.stack([jnp.stack(probs), jnp.stack(logs)], axis=1)
    result = lax.dynamic_slice_in_dim(result, bhi * pick, pick, 2)
    n_x = lax.axis_size("sx")
    back = result.reshape(n_x, n_sect // n_x, 2, pick)
    back = lax.all_to_all(back, "sy", 1, 1, tiled=False)
    back = lax.all_to_all(back, "sx", 0, 0, tiled=False).reshape(n_sect, 2, pick)
    out = jnp.transpose(back, (1, 0, 2)).reshape(2, bits.shape[0], n_sect * pick)
    return (out[0], out[1])


def solution(mesh):
    n_sect, n_blk = mesh.devices.shape
    n_x = n_sect // 2
    fine = Mesh(mesh.devices.reshape(n_x, 2, PARTS, n_blk // PARTS), ("sx", "sy", "bhi", "blo"))
    blk = ("bhi", "blo")
    in_specs = (P(SECT, blk), P(), P(blk, None), P(SECT, None, blk, None, None))
    out_specs = (P(SECT, blk), P(SECT, blk))
    return jax.shard_map(body, mesh=fine, in_specs=in_specs, out_specs=out_specs, check_vma=False)
```
